256 devices in a mesh: tm: 128 (over z, y, x), rows: 2 (over core).
Axes of the slice: x: 4, y: 4, z: 8, core: 2. Of those that a mesh axis runs over, the one named last changes fastest.
Arguments:
- band_blocks: float32 [8, 3, 64, 64], replicated, may hold values from 0.1 to 1
- band_offsets: int32 [8, 3], replicated, may hold values from 0 to 7, as said below
- retention: float32 [512], replicated, may hold values from 0.85 to 0.99
- frame_scale: float32 [512, 8], P('tm'), may hold values from 0.95 to 0.999
- sensor_index: int32 [128], replicated, may hold values from 0 to 511, as said below
- sensor_gain: float32 [128], replicated, may hold values from 0.2 to 0.6
- readings: float32 [512, 128], P('tm'), may hold values from -6 to 6
- noise_cov: float32 [512, 512], P(None, 'rows'), may hold values from -0.01 to 0.2
- initial_mean: float32 [512], replicated, may hold values from -6 to 6
- smoother_gain: float32 [512, 512], replicated, may hold values from -0.001 to 1, as said below
Outputs:
- filtered_cov: float32 [128, 512, 512], P('tm', None, 'rows')
- smoothed_means: float32 [512, 512], P('tm', 'rows')
The draws below stay inside these ranges and needn't reach their ends.
Inputs may be any that keep to these rules, and one draw needn't show every extreme that they name: `band_offsets`: band 0 of block row i names block i; the other bands of a row name distinct other blocks. `sensor_index`: the sensors read distinct nodes. Every eigenvalue of smoother_gain lies inside the unit circle.
All inputs are finite; a program needn't handle non-finite values.
Results may differ from the reference program's by a relative error of at most 0.0003.
Values sent between devices are 32-bit elements; how exact they have to be, the bound alone decides.
No kernel may reach another device: no remote copies, remote signals or barrier semaphores. Data moves between devices by JAX's collectives and lax.ppermute only.
A program may use at most 64 MiB of HBM per device.

```python
import jax
import jax.numpy as jnp
from jax import lax

N = 512
BLK = 64
BANDS = 3
S = 128
FR_DEV = 4
NB = 8
FRAMES = 512
N_TM = 128


def sensor_nodes(key):
    return jax.random.permutation(jax.random.fold_in(key, 11), N)[:S].astype(jnp.int32)


def draw_band_offsets(key, part):
    block_count = N // BLK
    row_keys = jax.random.split(jax.random.fold_in(key, 41), block_count)

    def one_row(row_key):
        return jax.random.permutation(row_key, block_count - 1)[:BANDS - 1] + 1
    shifts = jax.vmap(one_row)(row_keys).astype(jnp.int32)
    block_rows = jnp.arange(block_count, dtype=jnp.int32)[:, None]
    others = (block_rows + shifts) % block_count
    return jnp.concatenate([block_rows, others], axis=1).astype(jnp.int32)


def draw_sensor_index(key, part):
    return sensor_nodes(key)


def draw_retention(key, part):
    key_high = jax.random.fold_in(jax.random.fold_in(key, 61), 1)
    values = jax.random.uniform(key_high, (N,), jnp.float32, 0.85, 0.99)
    return values.astype(jnp.float32)


def draw_frame_scale(key, part):
    frame_key = jax.random.fold_in(key, 51)
    values = jax.random.uniform(frame_key, (FRAMES, N // BLK), jnp.float32, 0.95, 0.999)
    return values.astype(jnp.float32)


def draw_sensor_gain(key, part):
    gain_key = jax.random.fold_in(key, 71)
    values = jax.random.uniform(gain_key, (S,), jnp.float32, 0.2, 0.6)
    return values.astype(jnp.float32)


def draw_noise_cov(key, part):
    key_spread, key_diag = jax.random.split(jax.random.fold_in(key, 21))
    spread = jax.random.uniform(key_spread, (N, N), jnp.float32, -1.0, 1.0)
    offdiag = 0.75 * (spread + spread.T) / N
    identity = jnp.eye(N, dtype=jnp.float32)
    diagonal_part = jax.random.uniform(key_diag, (N,), jnp.float32, 1.6, 3.0)
    values = 0.03 * (offdiag * (1.0 - identity) + identity * diagonal_part[:, None])
    return values.astype(jnp.float32)


def draw_smoother_gain(key, part):
    key_spread, key_slow, key_fast, key_pick = jax.random.split(jax.random.fold_in(key, 31), 4)
    slow_rates = jax.random.uniform(key_slow, (N,), jnp.float32, 0.2, 2.0)
    slow_part = jnp.exp(-slow_rates / (1.0 * FRAMES))
    fast_lengths = jax.random.uniform(key_fast, (N,), jnp.float32, 20.0, 50.0)
    fast_part = jnp.exp(-1.0 / fast_lengths)
    picks = jax.random.randint(key_pick, (N,), 0, 10)
    slow_count = 5
    diagonal_part = jnp.where(picks < slow_count, slow_part, fast_part)
    spread = jax.random.uniform(key_spread, (N, N), jnp.float32, -1.0, 1.0)
    offdiag = spread * (0.5 * (1.0 - diagonal_part)[:, None] / N)
    identity = jnp.eye(N, dtype=jnp.float32)
    return (offdiag * (1.0 - identity) + identity * diagonal_part[:, None]).astype(jnp.float32)


def levels(stream_key, shape, cuts, smallest, high):
    def one(position, parts):
        draws = jax.random.uniform(jax.random.fold_in(jax.random.fold_in(stream_key, 6), position), (parts,), jnp.float32, smallest / len(cuts), high / len(cuts))
        return jnp.repeat(jnp.exp(draws), shape[position] // parts).reshape((-1,) + (1,) * (len(shape) - position - 1))

    factor_of = one(*cuts[0])
    for cut in cuts[1:]:
        factor_of = factor_of * one(*cut)
    return factor_of


def noise(stream_key, shape, deviation, bound, shards=(), kind=jnp.bfloat16):
    gain = levels(stream_key, shape, shards, -0.22, 0.18) if shards else 1.0
    values = jax.random.normal(stream_key, shape, jnp.float32) * deviation * gain
    return jnp.minimum(jnp.maximum(values, -bound), bound).astype(kind)


def setup_inputs(seed: int = 0) -> dict:
    keys = jax.random.split(jax.random.key(seed), 11)
    band_blocks = jnp.clip(jax.random.uniform(keys[0], (NB, BANDS, BLK, BLK), jnp.float32, 0.1, 1.0), 0.1, 1.0)
    band_offsets = draw_band_offsets(jax.random.fold_in(keys[10], 71), 0)
    retention = draw_retention(jax.random.fold_in(keys[10], 71), 0)
    frame_scale = draw_frame_scale(jax.random.fold_in(keys[10], 71), 0)
    sensor_index = draw_sensor_index(jax.random.fold_in(keys[10], 71), 0)
    sensor_gain = draw_sensor_gain(jax.random.fold_in(keys[10], 71), 0)
    readings = noise(keys[6], (FRAMES, S), 1.0, 6.0, ((0, 128),), jnp.float32)
    noise_cov = draw_noise_cov(jax.random.fold_in(keys[10], 71), 0)
    initial_mean = noise(keys[8], (N,), 1.0, 6.0, (), jnp.float32)
    smoother_gain = draw_smoother_gain(jax.random.fold_in(keys[10], 71), 0)
    return dict(band_blocks=band_blocks, band_offsets=band_offsets, retention=retention, frame_scale=frame_scale, sensor_index=sensor_index, sensor_gain=sensor_gain, readings=readings, noise_cov=noise_cov, initial_mean=initial_mean, smoother_gain=smoother_gain)


HIGHEST_PRECISION = lax.Precision.HIGHEST


def build_coupling(band_blocks, band_offsets, retention):
    block_count = band_blocks.shape[0]
    block_size = band_blocks.shape[2]
    totals = jnp.sum(band_blocks, axis=(1, 3))
    normed = band_blocks / totals[:, None, :, None]
    placement = (band_offsets[:, :, None] == jnp.arange(block_count, dtype=jnp.int32)[None, None, :]).astype(jnp.float32)
    spread_matrix = jnp.einsum("ibj,ibac->iajc", placement, normed, precision=HIGHEST_PRECISION)
    spread_matrix = spread_matrix.reshape(block_count * block_size, block_count * block_size)
    return (1.0 - retention)[:, None] * spread_matrix + jnp.diag(retention)


def reference(band_blocks, band_offsets, retention, frame_scale, sensor_index, sensor_gain, readings, noise_cov, initial_mean, smoother_gain):
    coupling = build_coupling(band_blocks, band_offsets, retention)
    node_count = coupling.shape[0]
    sensor_hit = (sensor_index[:, None] == jnp.arange(node_count, dtype=jnp.int32)[None, :]).astype(jnp.float32)
    damping = 1.0 - jnp.dot(sensor_gain, sensor_hit, precision=HIGHEST_PRECISION)
    inject = jnp.dot(readings * sensor_gain[None, :], sensor_hit, precision=HIGHEST_PRECISION)

    def frame_step(carry, inputs):
        mean_now, cov_now = carry
        scale_row, injected = inputs
        transition = jnp.repeat(scale_row, BLK)[:, None] * coupling
        predicted = jnp.dot(transition, mean_now, precision=HIGHEST_PRECISION)
        update = damping[:, None] * transition
        mean_now = damping * predicted + injected
        cov_now = jnp.dot(jnp.dot(update, cov_now, precision=HIGHEST_PRECISION), update.T, precision=HIGHEST_PRECISION) + noise_cov
        return (mean_now, cov_now), (mean_now, predicted)

    def segment_step(carry, inputs):
        carry, stacks = lax.scan(frame_step, carry, inputs)
        return carry, (stacks[0], stacks[1], carry[1])

    scales = frame_scale.reshape(N_TM, FR_DEV, frame_scale.shape[1])
    injects = inject.reshape(N_TM, FR_DEV, node_count)
    start = (initial_mean, jnp.zeros((node_count, node_count), jnp.float32))
    _, (mean_stack, pred_stack, covs) = lax.scan(segment_step, start, (scales, injects))
    mean_stack = mean_stack.reshape(FRAMES, node_count)
    pred_stack = pred_stack.reshape(FRAMES, node_count)
    pred_after = jnp.concatenate([pred_stack[1:], jnp.zeros((1, node_count), jnp.float32)], axis=0)

    def back_wrap(smooth_next, inputs):
        mean_now, pred_next, is_last = inputs
        bracket = jnp.where(is_last, jnp.zeros_like(smooth_next), smooth_next - pred_next)
        smooth = mean_now + jnp.dot(smoother_gain, bracket, precision=HIGHEST_PRECISION)
        return smooth, smooth

    last_flags = jnp.arange(FRAMES, dtype=jnp.int32) == FRAMES - 1
    _, smoothed = lax.scan(back_wrap, jnp.zeros((node_count,), jnp.float32), (mean_stack, pred_after, last_flags), reverse=True)
    return covs, smoothed
```

```python
import jax
import jax.numpy as jnp
from jax import lax
from jax.sharding import PartitionSpec as P

HIGHEST_PRECISION = lax.Precision.HIGHEST


def shifted(value, axis, steps):
    count = lax.axis_size(axis)
    leading, last = (max(0, -steps), min(count, count - steps))
    return lax.ppermute(value, axis, [(source, source + steps) for source in range(leading, last)])


def matmul(left, right):
    return jnp.dot(left, right, precision=HIGHEST_PRECISION, preferred_element_type=jnp.float32)


def full_columns(panel):
    count = lax.axis_size("rows")
    if count != 2:
        return lax.all_gather(panel, "rows", axis=1, tiled=True)
    other = lax.ppermute(panel, "rows", [(0, 1), (1, 0)])
    first = lax.axis_index("rows") == 0
    left = jnp.where(first, panel, other)
    right = jnp.where(first, other, panel)
    return jnp.concatenate([left, right], axis=1)


def build_coupling(band_blocks, band_offsets, retention):
    block_count = band_blocks.shape[0]
    block_size = band_blocks.shape[2]
    totals = jnp.sum(band_blocks, axis=(1, 3))
    normed = band_blocks / totals[:, None, :, None]
    placement = (
        band_offsets[:, :, None] == jnp.arange(block_count, dtype=jnp.int32)[None, None, :]
    ).astype(jnp.float32)
    spread_matrix = jnp.einsum("ibj,ibac->iajc", placement, normed, precision=HIGHEST_PRECISION)
    spread_matrix = spread_matrix.reshape(block_count * block_size, block_count * block_size)
    return (1.0 - retention)[:, None] * spread_matrix + jnp.diag(retention)


def matrix_power(square, exponent):
    result = None
    factor = square
    while exponent > 0:
        if exponent % 2 == 1:
            result = factor
        exponent = exponent // 2
        if exponent > 0:
            factor = matmul(factor, factor)
    return result


def local(
    band_blocks,
    band_offsets,
    retention,
    frame_scale,
    sensor_index,
    sensor_gain,
    readings,
    noise_cov,
    initial_mean,
    smoother_gain,
):
    node_count = retention.shape[0]
    block_size = band_blocks.shape[2]
    frames = readings.shape[0]
    panel_width = noise_cov.shape[1]
    tm_devices = lax.axis_size("tm")
    segment = lax.axis_index("tm")
    panel_start = lax.axis_index("rows") * panel_width
    coupling = build_coupling(band_blocks, band_offsets, retention)
    sensor_hit = (sensor_index[:, None] == jnp.arange(node_count, dtype=jnp.int32)[None, :]).astype(
        jnp.float32
    )
    damping = 1.0 - matmul(sensor_gain, sensor_hit)
    inject = matmul(readings * sensor_gain[None, :], sensor_hit)
    anchor = jnp.where(segment == 0, initial_mean, jnp.zeros_like(initial_mean))

    def transition(frame):
        scale_row = lax.dynamic_index_in_dim(frame_scale, frame, 0, keepdims=False)
        return jnp.repeat(scale_row, block_size)[:, None] * coupling

    def injected(frame):
        return lax.dynamic_index_in_dim(inject, frame, 0, keepdims=False)

    first_update = damping[:, None] * transition(0)
    first_offset = matmul(first_update, anchor) + inject[0]
    columns = (
        jnp.arange(node_count, dtype=jnp.int32)[:, None]
        == panel_start + jnp.arange(panel_width, dtype=jnp.int32)[None, :]
    ).astype(jnp.float32)

    def segment_frame(frame, carry):
        chain_cols, offset, cov_cols = carry
        update = damping[:, None] * transition(frame)
        gathered = full_columns(cov_cols)
        update_rows = lax.dynamic_slice_in_dim(update, panel_start, panel_width, 0)
        cov_cols = matmul(update, matmul(gathered, update_rows.T)) + noise_cov
        return (matmul(update, chain_cols), matmul(update, offset) + injected(frame), cov_cols)

    chain_cols, offset, cov_cols = lax.fori_loop(
        1, frames, segment_frame, (matmul(first_update, columns), first_offset, noise_cov)
    )

    offset_rows = offset.shape[0] // panel_width
    distances = [1 << level for level in range(tm_devices.bit_length()) if 1 << level < tm_devices]
    chain_full = full_columns(chain_cols)
    for position, stride in enumerate(distances):
        last = position == len(distances) - 1
        if last:
            sent = offset.reshape(offset_rows, panel_width)
        else:
            sent = jnp.concatenate([chain_cols, offset.reshape(offset_rows, panel_width)], axis=0)
        got = shifted(sent, "tm", stride)
        got_cov = shifted(cov_cols, "tm", stride)
        got_offset = got[got.shape[0] - offset_rows:].reshape(node_count)
        active = segment >= stride
        chain_rows = lax.dynamic_slice_in_dim(chain_full, panel_start, panel_width, 0)
        earlier_cov = full_columns(got_cov)
        new_cov = matmul(chain_full, matmul(earlier_cov, chain_rows.T)) + cov_cols
        new_offset = matmul(chain_full, got_offset) + offset
        cov_cols = jnp.where(active, new_cov, cov_cols)
        offset = jnp.where(active, new_offset, offset)
        if not last:
            new_chain = matmul(chain_full, got[: node_count])
            chain_cols = jnp.where(active, new_chain, chain_cols)
            chain_full = full_columns(chain_cols)
    cov_out = cov_cols[None]
    mean_start = jnp.where(segment == 0, initial_mean, shifted(offset, "tm", 1))

    def filter_frame(mean_now, frame):
        predicted = matmul(transition(frame), mean_now)
        mean_now = damping * predicted + injected(frame)
        return (mean_now, (mean_now, predicted))

    _, (mean_stack, pred_stack) = lax.scan(
        filter_frame, mean_start, jnp.arange(frames, dtype=jnp.int32)
    )

    def smooth_pass(bracket):

        def frame_back(bracket, inputs):
            mean_now, predicted = inputs
            smooth = mean_now + matmul(smoother_gain, bracket)
            return (smooth - predicted, smooth)

        return lax.scan(frame_back, bracket, (mean_stack, pred_stack), reverse=True)

    own_bracket, _ = smooth_pass(jnp.zeros_like(initial_mean))
    gain_power = matrix_power(smoother_gain, frames)
    suffix_distances = [1] + distances
    suffix = own_bracket
    for position, stride in enumerate(suffix_distances):
        received = shifted(suffix, "tm", -stride)
        if position == 0:
            suffix = received
        else:
            suffix = suffix + matmul(gain_power, received)
            gain_power = matmul(gain_power, gain_power)
    _, smoothed = smooth_pass(suffix)
    return (cov_out, lax.dynamic_slice_in_dim(smoothed, panel_start, panel_width, 1))


def solution(mesh):
    return jax.shard_map(
        local,
        mesh=mesh,
        in_specs=(P(), P(), P(), P("tm", None), P(), P(), P("tm", None), P(None, "rows"), P(), P()),
        out_specs=(P("tm", None, "rows"), P("tm", "rows")),
        check_vma=False,
    )
```

```python
import jax
import jax.numpy as jnp
from jax import lax
from jax.sharding import PartitionSpec as P

HIGHEST_PRECISION = lax.Precision.HIGHEST


def shifted(value, axis, steps):
    count = lax.axis_size(axis)
    leading, last = (max(0, -steps), min(count, count - steps))
    return lax.ppermute(value, axis, [(source, source + steps) for source in range(leading, last)])


def matmul(left, right):
    return jnp.dot(left, right, precision=HIGHEST_PRECISION, preferred_element_type=jnp.float32)


def full_columns(panel):
    count = lax.axis_size("rows")
    if count != 2:
        return lax.all_gather(panel, "rows", axis=1, tiled=True)
    other = lax.ppermute(panel, "rows", [(0, 1), (1, 0)])
    first = lax.axis_index("rows") == 0
    left = jnp.where(first, panel, other)
    right = jnp.where(first, other, panel)
    return jnp.concatenate([left, right], axis=1)


def build_coupling(band_blocks, band_offsets, retention):
    block_count = band_blocks.shape[0]
    block_size = band_blocks.shape[2]
    totals = jnp.sum(band_blocks, axis=(1, 3))
    normed = band_blocks / totals[:, None, :, None]
    placement = (
        band_offsets[:, :, None] == jnp.arange(block_count, dtype=jnp.int32)[None, None, :]
    ).astype(jnp.float32)
    spread_matrix = jnp.einsum("ibj,ibac->iajc", placement, normed, precision=HIGHEST_PRECISION)
    spread_matrix = spread_matrix.reshape(block_count * block_size, block_count * block_size)
    return (1.0 - retention)[:, None] * spread_matrix + jnp.diag(retention)


def matrix_power(square, exponent):
    result = None
    factor = square
    while exponent > 0:
        if exponent % 2 == 1:
            result = factor
        exponent = exponent // 2
        if exponent > 0:
            factor = matmul(factor, factor)
    return result


def local(
    band_blocks,
    band_offsets,
    retention,
    frame_scale,
    sensor_index,
    sensor_gain,
    readings,
    noise_cov,
    initial_mean,
    smoother_gain,
):
    node_count = retention.shape[0]
    block_size = band_blocks.shape[2]
    frames = readings.shape[0]
    panel_width = noise_cov.shape[1]
    tm_devices = lax.axis_size("tm")
    segment = lax.axis_index("tm")
    panel_start = lax.axis_index("rows") * panel_width
    coupling = build_coupling(band_blocks, band_offsets, retention)
    sensor_hit = (sensor_index[:, None] == jnp.arange(node_count, dtype=jnp.int32)[None, :]).astype(
        jnp.float32
    )
    damping = 1.0 - matmul(sensor_gain, sensor_hit)
    inject = matmul(readings * sensor_gain[None, :], sensor_hit)
    anchor = jnp.where(segment == 0, initial_mean, jnp.zeros_like(initial_mean))

    def transition(frame):
        scale_row = lax.dynamic_index_in_dim(frame_scale, frame, 0, keepdims=False)
        return jnp.repeat(scale_row, block_size)[:, None] * coupling

    def injected(frame):
        return lax.dynamic_index_in_dim(inject, frame, 0, keepdims=False)

    first_update = damping[:, None] * transition(0)
    first_offset = matmul(first_update, anchor) + inject[0]
    columns = (
        jnp.arange(node_count, dtype=jnp.int32)[:, None]
        == panel_start + jnp.arange(panel_width, dtype=jnp.int32)[None, :]
    ).astype(jnp.float32)

    def segment_frame(frame, carry):
        chain_cols, offset, cov_cols = carry
        update = damping[:, None] * transition(frame)
        gathered = full_columns(cov_cols)
        update_rows = lax.dynamic_slice_in_dim(update, panel_start, panel_width, 0)
        cov_cols = matmul(update, matmul(gathered, update_rows.T)) + noise_cov
        return (matmul(update, chain_cols), matmul(update, offset) + injected(frame), cov_cols)

    chain_cols, offset, cov_cols = lax.fori_loop(
        1, frames, segment_frame, (matmul(first_update, columns), first_offset, noise_cov)
    )

    offset_rows = offset.shape[0] // panel_width
    distances = [1 << level for level in range(tm_devices.bit_length()) if 1 << level < tm_devices]
    chain_full = full_columns(chain_cols)
    for position, stride in enumerate(distances):
        last = position == len(distances) - 1
        if last:
            sent = offset.reshape(offset_rows, panel_width)
        else:
            sent = jnp.concatenate([chain_cols, offset.reshape(offset_rows, panel_width)], axis=0)
        got = shifted(sent, "tm", stride)
        cov_send, got = lax.optimization_barrier((cov_cols, got))
        got_cov = shifted(cov_send, "tm", stride)
        got_offset = got[got.shape[0] - offset_rows:].reshape(node_count)
        active = segment >= stride
        chain_rows = lax.dynamic_slice_in_dim(chain_full, panel_start, panel_width, 0)
        earlier_cov = full_columns(got_cov)
        new_cov = matmul(chain_full, matmul(earlier_cov, chain_rows.T)) + cov_cols
        new_offset = matmul(chain_full, got_offset) + offset
        cov_cols = jnp.where(active, new_cov, cov_cols)
        offset = jnp.where(active, new_offset, offset)
        if not last:
            new_chain = matmul(chain_full, got[: node_count])
            chain_cols = jnp.where(active, new_chain, chain_cols)
            chain_full = full_columns(chain_cols)
    cov_out = cov_cols[None]
    mean_start = jnp.where(segment == 0, initial_mean, shifted(offset, "tm", 1))

    scale_rows = jnp.repeat(frame_scale, block_size, axis=1)
    mean_stack = []
    pred_stack = []
    mean_now = mean_start
    for frame in range(frames):
        predicted = scale_rows[frame] * matmul(coupling, mean_now)
        mean_now = damping * predicted + inject[frame]
        mean_stack.append(mean_now)
        pred_stack.append(predicted)

    def smooth_pass(bracket):
        smooth = [None] * frames
        for frame in reversed(range(frames)):
            smooth[frame] = mean_stack[frame] + matmul(smoother_gain, bracket)
            bracket = smooth[frame] - pred_stack[frame]
        return bracket, jnp.stack(smooth)

    own_bracket, _ = smooth_pass(jnp.zeros_like(initial_mean))
    brackets = lax.all_gather(own_bracket, "tm")
    gain_power = matrix_power(smoother_gain, frames)
    total = brackets
    for stride in distances:
        later = jnp.concatenate(
            [total[stride:], jnp.zeros((stride, node_count), jnp.float32)], axis=0
        )
        total = total + lax.dot_general(
            later, gain_power, (((1,), (1,)), ((), ())),
            precision=HIGHEST_PRECISION, preferred_element_type=jnp.float32,
        )
        gain_power = matmul(gain_power, gain_power)
    following = lax.dynamic_index_in_dim(
        total, jnp.minimum(segment + 1, tm_devices - 1), 0, keepdims=False
    )
    suffix = jnp.where(segment == tm_devices - 1, jnp.zeros_like(following), following)
    _, smoothed = smooth_pass(suffix)
    return (cov_out, lax.dynamic_slice_in_dim(smoothed, panel_start, panel_width, 1))


def solution(mesh):
    return jax.shard_map(
        local,
        mesh=mesh,
        in_specs=(P(), P(), P(), P("tm", None), P(), P(), P("tm", None), P(None, "rows"), P(), P()),
        out_specs=(P("tm", None, "rows"), P("tm", "rows")),
        check_vma=False,
    )
```

```python
import jax
import jax.numpy as jnp
from jax import lax
from jax.sharding import PartitionSpec as P

HIGHEST_PRECISION = lax.Precision.HIGHEST


def shifted(value, axis, steps):
    count = lax.axis_size(axis)
    leading, last = (max(0, -steps), min(count, count - steps))
    return lax.ppermute(value, axis, [(source, source + steps) for source in range(leading, last)])


def matmul(left, right):
    return jnp.dot(left, right, precision=HIGHEST_PRECISION, preferred_element_type=jnp.float32)


def full_columns(panel):
    count = lax.axis_size("rows")
    if count != 2:
        return lax.all_gather(panel, "rows", axis=1, tiled=True)
    other = lax.ppermute(panel, "rows", [(0, 1), (1, 0)])
    first = lax.axis_index("rows") == 0
    left = jnp.where(first, panel, other)
    right = jnp.where(first, other, panel)
    return jnp.concatenate([left, right], axis=1)


def build_coupling(band_blocks, band_offsets, retention):
    block_count = band_blocks.shape[0]
    block_size = band_blocks.shape[2]
    totals = jnp.sum(band_blocks, axis=(1, 3))
    normed = band_blocks / totals[:, None, :, None]
    placement = (
        band_offsets[:, :, None] == jnp.arange(block_count, dtype=jnp.int32)[None, None, :]
    ).astype(jnp.float32)
    spread_matrix = jnp.einsum("ibj,ibac->iajc", placement, normed, precision=HIGHEST_PRECISION)
    spread_matrix = spread_matrix.reshape(block_count * block_size, block_count * block_size)
    return (1.0 - retention)[:, None] * spread_matrix + jnp.diag(retention)


def matrix_power(square, exponent):
    result = None
    factor = square
    while exponent > 0:
        if exponent % 2 == 1:
            result = factor
        exponent = exponent // 2
        if exponent > 0:
            factor = matmul(factor, factor)
    return result


def local(
    band_blocks,
    band_offsets,
    retention,
    frame_scale,
    sensor_index,
    sensor_gain,
    readings,
    noise_cov,
    initial_mean,
    smoother_gain,
):
    node_count = retention.shape[0]
    block_size = band_blocks.shape[2]
    frames = readings.shape[0]
    panel_width = noise_cov.shape[1]
    tm_devices = lax.axis_size("tm")
    segment = lax.axis_index("tm")
    panel_start = lax.axis_index("rows") * panel_width
    coupling = build_coupling(band_blocks, band_offsets, retention)
    sensor_hit = (sensor_index[:, None] == jnp.arange(node_count, dtype=jnp.int32)[None, :]).astype(
        jnp.float32
    )
    damping = 1.0 - matmul(sensor_gain, sensor_hit)
    inject = matmul(readings * sensor_gain[None, :], sensor_hit)
    anchor = jnp.where(segment == 0, initial_mean, jnp.zeros_like(initial_mean))

    def transition(frame):
        scale_row = lax.dynamic_index_in_dim(frame_scale, frame, 0, keepdims=False)
        return jnp.repeat(scale_row, block_size)[:, None] * coupling

    def injected(frame):
        return lax.dynamic_index_in_dim(inject, frame, 0, keepdims=False)

    first_update = damping[:, None] * transition(0)
    first_offset = matmul(first_update, anchor) + inject[0]
    columns = (
        jnp.arange(node_count, dtype=jnp.int32)[:, None]
        == panel_start + jnp.arange(panel_width, dtype=jnp.int32)[None, :]
    ).astype(jnp.float32)

    def segment_frame(frame, carry):
        chain_cols, offset, cov_cols = carry
        update = damping[:, None] * transition(frame)
        gathered = full_columns(cov_cols)
        update_rows = lax.dynamic_slice_in_dim(update, panel_start, panel_width, 0)
        cov_cols = matmul(update, matmul(gathered, update_rows.T)) + noise_cov
        return (matmul(update, chain_cols), matmul(update, offset) + injected(frame), cov_cols)

    chain_cols, offset, cov_cols = lax.fori_loop(
        1, frames, segment_frame, (matmul(first_update, columns), first_offset, noise_cov)
    )

    offset_rows = offset.shape[0] // panel_width
    distances = [1 << level for level in range(tm_devices.bit_length()) if 1 << level < tm_devices]
    chain_full = full_columns(chain_cols)
    cov_history = []
    for position, stride in enumerate(distances):
        last = position == len(distances) - 1
        if last:
            sent = offset.reshape(offset_rows, panel_width)
        else:
            sent = jnp.concatenate([chain_cols, offset.reshape(offset_rows, panel_width)], axis=0)
        if position >= 2:
            sent, _ = lax.optimization_barrier((sent, cov_history[position - 1]))
        cov_history.append(cov_cols)
        got = shifted(sent, "tm", stride)
        cov_send, got = lax.optimization_barrier((cov_cols, got))
        got_cov = shifted(cov_send, "tm", stride)
        got_offset = got[got.shape[0] - offset_rows:].reshape(node_count)
        active = segment >= stride
        chain_rows = lax.dynamic_slice_in_dim(chain_full, panel_start, panel_width, 0)
        earlier_cov = full_columns(got_cov)
        new_cov = matmul(chain_full, matmul(earlier_cov, chain_rows.T)) + cov_cols
        new_offset = matmul(chain_full, got_offset) + offset
        cov_cols = jnp.where(active, new_cov, cov_cols)
        offset = jnp.where(active, new_offset, offset)
        if not last:
            new_chain = matmul(chain_full, got[: node_count])
            chain_cols = jnp.where(active, new_chain, chain_cols)
            chain_full = full_columns(chain_cols)
    cov_out = cov_cols[None]
    mean_start = jnp.where(segment == 0, initial_mean, shifted(offset, "tm", 1))

    scale_rows = jnp.repeat(frame_scale, block_size, axis=1)
    mean_stack = []
    pred_stack = []
    mean_now = mean_start
    for frame in range(frames):
        predicted = scale_rows[frame] * matmul(coupling, mean_now)
        mean_now = damping * predicted + inject[frame]
        mean_stack.append(mean_now)
        pred_stack.append(predicted)

    def smooth_pass(bracket):
        smooth = [None] * frames
        for frame in reversed(range(frames)):
            smooth[frame] = mean_stack[frame] + matmul(smoother_gain, bracket)
            bracket = smooth[frame] - pred_stack[frame]
        return bracket, jnp.stack(smooth)

    own_bracket, _ = smooth_pass(jnp.zeros_like(initial_mean))
    squares = [matrix_power(smoother_gain, frames)]
    powers = {}

    def power(exponent):
        if exponent not in powers:
            result = None
            bit = 0
            while exponent >> bit:
                while len(squares) <= bit:
                    squares.append(matmul(squares[-1], squares[-1]))
                if (exponent >> bit) & 1:
                    result = squares[bit] if result is None else matmul(result, squares[bit])
                bit += 1
            powers[exponent] = result
        return powers[exponent]

    suffix = None
    for step in range(1, 5):
        if step < tm_devices:
            term = shifted(own_bracket, "tm", -step)
            if step > 1:
                term = matmul(power(step - 1), term)
            suffix = term if suffix is None else suffix + term
    width = 4
    while width < tm_devices - 1:
        terms = []
        for multiple in range(1, 4):
            if multiple * width < tm_devices:
                terms.append((multiple * width, shifted(suffix, "tm", -multiple * width)))
        for stride, received in terms:
            suffix = suffix + matmul(power(stride), received)
        width *= 4
    _, smoothed = smooth_pass(suffix)
    return (cov_out, lax.dynamic_slice_in_dim(smoothed, panel_start, panel_width, 1))


def solution(mesh):
    return jax.shard_map(
        local,
        mesh=mesh,
        in_specs=(P(), P(), P(), P("tm", None), P(), P(), P("tm", None), P(None, "rows"), P(), P()),
        out_specs=(P("tm", None, "rows"), P("tm", "rows")),
        check_vma=False,
    )
```

```python
import jax
import jax.numpy as jnp
from jax import lax
from jax.sharding import PartitionSpec as P

HIGHEST_PRECISION = lax.Precision.HIGHEST


def shifted(value, axis, steps):
    count = lax.axis_size(axis)
    leading, last = (max(0, -steps), min(count, count - steps))
    return lax.ppermute(value, axis, [(source, source + steps) for source in range(leading, last)])


def matmul(left, right):
    return jnp.dot(left, right, precision=HIGHEST_PRECISION, preferred_element_type=jnp.float32)


def full_columns(panel):
    count = lax.axis_size("rows")
    if count != 2:
        return lax.all_gather(panel, "rows", axis=1, tiled=True)
    other = lax.ppermute(panel, "rows", [(0, 1), (1, 0)])
    first = lax.axis_index("rows") == 0
    left = jnp.where(first, panel, other)
    right = jnp.where(first, other, panel)
    return jnp.concatenate([left, right], axis=1)


def build_coupling(band_blocks, band_offsets, retention):
    block_count = band_blocks.shape[0]
    block_size = band_blocks.shape[2]
    totals = jnp.sum(band_blocks, axis=(1, 3))
    normed = band_blocks / totals[:, None, :, None]
    placement = (
        band_offsets[:, :, None] == jnp.arange(block_count, dtype=jnp.int32)[None, None, :]
    ).astype(jnp.float32)
    spread_matrix = jnp.einsum("ibj,ibac->iajc", placement, normed, precision=HIGHEST_PRECISION)
    spread_matrix = spread_matrix.reshape(block_count * block_size, block_count * block_size)
    return (1.0 - retention)[:, None] * spread_matrix + jnp.diag(retention)


def matrix_power(square, exponent):
    result = None
    factor = square
    while exponent > 0:
        if exponent % 2 == 1:
            result = factor
        exponent = exponent // 2
        if exponent > 0:
            factor = matmul(factor, factor)
    return result


def local(
    band_blocks,
    band_offsets,
    retention,
    frame_scale,
    sensor_index,
    sensor_gain,
    readings,
    noise_cov,
    initial_mean,
    smoother_gain,
):
    node_count = retention.shape[0]
    block_size = band_blocks.shape[2]
    frames = readings.shape[0]
    panel_width = noise_cov.shape[1]
    tm_devices = lax.axis_size("tm")
    segment = lax.axis_index("tm")
    panel_start = lax.axis_index("rows") * panel_width
    coupling = build_coupling(band_blocks, band_offsets, retention)
    sensor_hit = (sensor_index[:, None] == jnp.arange(node_count, dtype=jnp.int32)[None, :]).astype(
        jnp.float32
    )
    damping = 1.0 - matmul(sensor_gain, sensor_hit)
    inject = matmul(readings * sensor_gain[None, :], sensor_hit)
    anchor = jnp.where(segment == 0, initial_mean, jnp.zeros_like(initial_mean))

    def transition(frame):
        scale_row = lax.dynamic_index_in_dim(frame_scale, frame, 0, keepdims=False)
        return jnp.repeat(scale_row, block_size)[:, None] * coupling

    def injected(frame):
        return lax.dynamic_index_in_dim(inject, frame, 0, keepdims=False)

    first_update = damping[:, None] * transition(0)
    first_offset = matmul(first_update, anchor) + inject[0]
    columns = (
        jnp.arange(node_count, dtype=jnp.int32)[:, None]
        == panel_start + jnp.arange(panel_width, dtype=jnp.int32)[None, :]
    ).astype(jnp.float32)

    def segment_frame(frame, carry):
        chain_cols, offset, cov_cols = carry
        update = damping[:, None] * transition(frame)
        gathered = full_columns(cov_cols)
        update_rows = lax.dynamic_slice_in_dim(update, panel_start, panel_width, 0)
        cov_cols = matmul(update, matmul(gathered, update_rows.T)) + noise_cov
        return (matmul(update, chain_cols), matmul(update, offset) + injected(frame), cov_cols)

    chain_cols, offset, cov_cols = lax.fori_loop(
        1, frames, segment_frame, (matmul(first_update, columns), first_offset, noise_cov)
    )

    offset_rows = offset.shape[0] // panel_width
    distances = [1 << level for level in range(tm_devices.bit_length()) if 1 << level < tm_devices]
    chain_full = full_columns(chain_cols)
    for position, stride in enumerate(distances):
        last = position == len(distances) - 1
        if last:
            sent = offset.reshape(offset_rows, panel_width)
        else:
            sent = jnp.concatenate([chain_cols, offset.reshape(offset_rows, panel_width)], axis=0)
        got = shifted(sent, "tm", stride)
        got_cov = shifted(cov_cols, "tm", stride)
        got_offset = got[got.shape[0] - offset_rows:].reshape(node_count)
        active = segment >= stride
        chain_rows = lax.dynamic_slice_in_dim(chain_full, panel_start, panel_width, 0)
        earlier_cov = full_columns(got_cov)
        new_cov = matmul(chain_full, matmul(earlier_cov, chain_rows.T)) + cov_cols
        new_offset = matmul(chain_full, got_offset) + offset
        cov_cols = jnp.where(active, new_cov, cov_cols)
        offset = jnp.where(active, new_offset, offset)
        if not last:
            new_chain = matmul(chain_full, got[: node_count])
            chain_cols = jnp.where(active, new_chain, chain_cols)
            chain_full = full_columns(chain_cols)
    cov_out = cov_cols[None]
    mean_start = jnp.where(segment == 0, initial_mean, shifted(offset, "tm", 1))

    scale_rows = jnp.repeat(frame_scale, block_size, axis=1)
    mean_stack = []
    pred_stack = []
    mean_now = mean_start
    for frame in range(frames):
        predicted = scale_rows[frame] * matmul(coupling, mean_now)
        mean_now = damping * predicted + inject[frame]
        mean_stack.append(mean_now)
        pred_stack.append(predicted)

    def smooth_pass(bracket):
        smooth = [None] * frames
        for frame in reversed(range(frames)):
            smooth[frame] = mean_stack[frame] + matmul(smoother_gain, bracket)
            bracket = smooth[frame] - pred_stack[frame]
        return bracket, jnp.stack(smooth)

    own_bracket, _ = smooth_pass(jnp.zeros_like(initial_mean))
    squares = [matrix_power(smoother_gain, frames)]
    powers = {}

    def power(exponent):
        if exponent not in powers:
            result = None
            bit = 0
            while exponent >> bit:
                while len(squares) <= bit:
                    squares.append(matmul(squares[-1], squares[-1]))
                if (exponent >> bit) & 1:
                    result = squares[bit] if result is None else matmul(result, squares[bit])
                bit += 1
            powers[exponent] = result
        return powers[exponent]

    suffix = None
    for step in range(1, 5):
        if step < tm_devices:
            term = shifted(own_bracket, "tm", -step)
            if step > 1:
                term = matmul(power(step - 1), term)
            suffix = term if suffix is None else suffix + term
    width = 4
    while width < tm_devices - 1:
        terms = []
        for multiple in range(1, 4):
            if multiple * width < tm_devices:
                terms.append((multiple * width, shifted(suffix, "tm", -multiple * width)))
        for stride, received in terms:
            suffix = suffix + matmul(power(stride), received)
        width *= 4
    _, smoothed = smooth_pass(suffix)
    return (cov_out, lax.dynamic_slice_in_dim(smoothed, panel_start, panel_width, 1))


def solution(mesh):
    return jax.shard_map(
        local,
        mesh=mesh,
        in_specs=(P(), P(), P(), P("tm", None), P(), P(), P("tm", None), P(None, "rows"), P(), P()),
        out_specs=(P("tm", None, "rows"), P("tm", "rows")),
        check_vma=False,
    )
```

```python
import jax
import jax.numpy as jnp
from jax import lax
from jax.sharding import PartitionSpec as P

HIGHEST_PRECISION = lax.Precision.HIGHEST


def shifted(value, axis, steps):
    count = lax.axis_size(axis)
    leading, last = (max(0, -steps), min(count, count - steps))
    return lax.ppermute(value, axis, [(source, source + steps) for source in range(leading, last)])


def matmul(left, right):
    return jnp.dot(left, right, precision=HIGHEST_PRECISION, preferred_element_type=jnp.float32)


def matvec(square, vector):
    return jnp.sum(square * vector[None, :], axis=1)


def full_columns(panel):
    count = lax.axis_size("rows")
    if count != 2:
        return lax.all_gather(panel, "rows", axis=1, tiled=True)
    other = lax.ppermute(panel, "rows", [(0, 1), (1, 0)])
    first = lax.axis_index("rows") == 0
    left = jnp.where(first, panel, other)
    right = jnp.where(first, other, panel)
    return jnp.concatenate([left, right], axis=1)


def build_coupling(band_blocks, band_offsets, retention):
    block_count = band_blocks.shape[0]
    block_size = band_blocks.shape[2]
    totals = jnp.sum(band_blocks, axis=(1, 3))
    normed = band_blocks / totals[:, None, :, None]
    placement = (
        band_offsets[:, :, None] == jnp.arange(block_count, dtype=jnp.int32)[None, None, :]
    ).astype(jnp.float32)
    spread_matrix = jnp.einsum("ibj,ibac->iajc", placement, normed, precision=HIGHEST_PRECISION)
    spread_matrix = spread_matrix.reshape(block_count * block_size, block_count * block_size)
    return (1.0 - retention)[:, None] * spread_matrix + jnp.diag(retention)


def matrix_power(square, exponent):
    result = None
    factor = square
    while exponent > 0:
        if exponent % 2 == 1:
            result = factor
        exponent = exponent // 2
        if exponent > 0:
            factor = matmul(factor, factor)
    return result


def local(
    band_blocks,
    band_offsets,
    retention,
    frame_scale,
    sensor_index,
    sensor_gain,
    readings,
    noise_cov,
    initial_mean,
    smoother_gain,
):
    node_count = retention.shape[0]
    block_size = band_blocks.shape[2]
    frames = readings.shape[0]
    panel_width = noise_cov.shape[1]
    tm_devices = lax.axis_size("tm")
    segment = lax.axis_index("tm")
    panel_start = lax.axis_index("rows") * panel_width
    coupling = build_coupling(band_blocks, band_offsets, retention)
    sensor_hit = (sensor_index[:, None] == jnp.arange(node_count, dtype=jnp.int32)[None, :]).astype(
        jnp.float32
    )
    damping = 1.0 - matmul(sensor_gain, sensor_hit)
    inject = matmul(readings * sensor_gain[None, :], sensor_hit)
    anchor = jnp.where(segment == 0, initial_mean, jnp.zeros_like(initial_mean))

    def transition(frame):
        scale_row = lax.dynamic_index_in_dim(frame_scale, frame, 0, keepdims=False)
        return jnp.repeat(scale_row, block_size)[:, None] * coupling

    def injected(frame):
        return lax.dynamic_index_in_dim(inject, frame, 0, keepdims=False)

    first_update = damping[:, None] * transition(0)
    first_offset = matmul(first_update, anchor) + inject[0]
    columns = (
        jnp.arange(node_count, dtype=jnp.int32)[:, None]
        == panel_start + jnp.arange(panel_width, dtype=jnp.int32)[None, :]
    ).astype(jnp.float32)

    def segment_frame(frame, carry):
        chain_cols, offset, cov_cols = carry
        update = damping[:, None] * transition(frame)
        gathered = full_columns(cov_cols)
        update_rows = lax.dynamic_slice_in_dim(update, panel_start, panel_width, 0)
        cov_cols = matmul(update, matmul(gathered, update_rows.T)) + noise_cov
        return (matmul(update, chain_cols), matmul(update, offset) + injected(frame), cov_cols)

    chain_cols, offset, cov_cols = lax.fori_loop(
        1, frames, segment_frame, (matmul(first_update, columns), first_offset, noise_cov)
    )

    offset_rows = offset.shape[0] // panel_width
    distances = [1 << level for level in range(tm_devices.bit_length()) if 1 << level < tm_devices]
    chain_full = full_columns(chain_cols)
    for position, stride in enumerate(distances):
        last = position == len(distances) - 1
        if last:
            sent = offset.reshape(offset_rows, panel_width)
        else:
            sent = jnp.concatenate([chain_cols, offset.reshape(offset_rows, panel_width)], axis=0)
        got = shifted(sent, "tm", stride)
        got_cov = shifted(cov_cols, "tm", stride)
        got_offset = got[got.shape[0] - offset_rows:].reshape(node_count)
        active = segment >= stride
        chain_rows = lax.dynamic_slice_in_dim(chain_full, panel_start, panel_width, 0)
        earlier_cov = full_columns(got_cov)
        new_cov = matmul(chain_full, matmul(earlier_cov, chain_rows.T)) + cov_cols
        new_offset = matvec(chain_full, got_offset) + offset
        cov_cols = jnp.where(active, new_cov, cov_cols)
        offset = jnp.where(active, new_offset, offset)
        if not last:
            new_chain = matmul(chain_full, got[: node_count])
            chain_cols = jnp.where(active, new_chain, chain_cols)
            chain_full = full_columns(chain_cols)
    cov_out = cov_cols[None]
    mean_start = jnp.where(segment == 0, initial_mean, shifted(offset, "tm", 1))

    scale_rows = jnp.repeat(frame_scale, block_size, axis=1)
    mean_stack = []
    pred_stack = []
    mean_now = mean_start
    for frame in range(frames):
        predicted = scale_rows[frame] * matvec(coupling, mean_now)
        mean_now = damping * predicted + inject[frame]
        mean_stack.append(mean_now)
        pred_stack.append(predicted)

    def smooth_pass(bracket):
        smooth = [None] * frames
        for frame in reversed(range(frames)):
            smooth[frame] = mean_stack[frame] + matvec(smoother_gain, bracket)
            bracket = smooth[frame] - pred_stack[frame]
        return bracket, jnp.stack(smooth)

    own_bracket, _ = smooth_pass(jnp.zeros_like(initial_mean))
    squares = [matrix_power(smoother_gain, frames)]
    powers = {}

    def power(exponent):
        if exponent not in powers:
            result = None
            bit = 0
            while exponent >> bit:
                while len(squares) <= bit:
                    squares.append(matmul(squares[-1], squares[-1]))
                if (exponent >> bit) & 1:
                    result = squares[bit] if result is None else matmul(result, squares[bit])
                bit += 1
            powers[exponent] = result
        return powers[exponent]

    suffix = None
    for step in range(1, 5):
        if step < tm_devices:
            term = shifted(own_bracket, "tm", -step)
            if step > 1:
                term = matvec(power(step - 1), term)
            suffix = term if suffix is None else suffix + term
    width = 4
    while width < tm_devices - 1:
        terms = []
        for multiple in range(1, 4):
            if multiple * width < tm_devices:
                terms.append((multiple * width, shifted(suffix, "tm", -multiple * width)))
        for stride, received in terms:
            suffix = suffix + matvec(power(stride), received)
        width *= 4
    _, smoothed = smooth_pass(suffix)
    return (cov_out, lax.dynamic_slice_in_dim(smoothed, panel_start, panel_width, 1))


def solution(mesh):
    return jax.shard_map(
        local,
        mesh=mesh,
        in_specs=(P(), P(), P(), P("tm", None), P(), P(), P("tm", None), P(None, "rows"), P(), P()),
        out_specs=(P("tm", None, "rows"), P("tm", "rows")),
        check_vma=False,
    )
```

```python
import jax
import jax.numpy as jnp
from jax import lax
from jax.sharding import PartitionSpec as P

HIGHEST_PRECISION = lax.Precision.HIGHEST


def shifted(value, axis, steps):
    count = lax.axis_size(axis)
    leading, last = (max(0, -steps), min(count, count - steps))
    return lax.ppermute(value, axis, [(source, source + steps) for source in range(leading, last)])


def matmul(left, right):
    return jnp.dot(left, right, precision=HIGHEST_PRECISION, preferred_element_type=jnp.float32)


def full_columns(panel):
    count = lax.axis_size("rows")
    if count != 2:
        return lax.all_gather(panel, "rows", axis=1, tiled=True)
    other = lax.ppermute(panel, "rows", [(0, 1), (1, 0)])
    first = lax.axis_index("rows") == 0
    left = jnp.where(first, panel, other)
    right = jnp.where(first, other, panel)
    return jnp.concatenate([left, right], axis=1)


def build_coupling(band_blocks, band_offsets, retention):
    block_count = band_blocks.shape[0]
    block_size = band_blocks.shape[2]
    totals = jnp.sum(band_blocks, axis=(1, 3))
    normed = band_blocks / totals[:, None, :, None]
    placement = (
        band_offsets[:, :, None] == jnp.arange(block_count, dtype=jnp.int32)[None, None, :]
    ).astype(jnp.float32)
    spread_matrix = jnp.einsum("ibj,ibac->iajc", placement, normed, precision=HIGHEST_PRECISION)
    spread_matrix = spread_matrix.reshape(block_count * block_size, block_count * block_size)
    return (1.0 - retention)[:, None] * spread_matrix + jnp.diag(retention)


def matrix_power(square, exponent):
    result = None
    factor = square
    while exponent > 0:
        if exponent % 2 == 1:
            result = factor
        exponent = exponent // 2
        if exponent > 0:
            factor = matmul(factor, factor)
    return result


def local(
    band_blocks,
    band_offsets,
    retention,
    frame_scale,
    sensor_index,
    sensor_gain,
    readings,
    noise_cov,
    initial_mean,
    smoother_gain,
):
    node_count = retention.shape[0]
    block_size = band_blocks.shape[2]
    frames = readings.shape[0]
    panel_width = noise_cov.shape[1]
    tm_devices = lax.axis_size("tm")
    segment = lax.axis_index("tm")
    panel_start = lax.axis_index("rows") * panel_width
    coupling = build_coupling(band_blocks, band_offsets, retention)
    sensor_hit = (sensor_index[:, None] == jnp.arange(node_count, dtype=jnp.int32)[None, :]).astype(
        jnp.float32
    )
    damping = 1.0 - matmul(sensor_gain, sensor_hit)
    inject = matmul(readings * sensor_gain[None, :], sensor_hit)
    anchor = jnp.where(segment == 0, initial_mean, jnp.zeros_like(initial_mean))

    def transition(frame):
        scale_row = lax.dynamic_index_in_dim(frame_scale, frame, 0, keepdims=False)
        return jnp.repeat(scale_row, block_size)[:, None] * coupling

    def injected(frame):
        return lax.dynamic_index_in_dim(inject, frame, 0, keepdims=False)

    first_update = damping[:, None] * transition(0)
    first_offset = matmul(first_update, anchor) + inject[0]
    columns = (
        jnp.arange(node_count, dtype=jnp.int32)[:, None]
        == panel_start + jnp.arange(panel_width, dtype=jnp.int32)[None, :]
    ).astype(jnp.float32)

    def segment_frame(frame, carry):
        chain_cols, offset, cov_cols = carry
        update = damping[:, None] * transition(frame)
        gathered = full_columns(cov_cols)
        update_rows = lax.dynamic_slice_in_dim(update, panel_start, panel_width, 0)
        cov_cols = matmul(update, matmul(gathered, update_rows.T)) + noise_cov
        return (matmul(update, chain_cols), matmul(update, offset) + injected(frame), cov_cols)

    chain_cols, offset, cov_cols = lax.fori_loop(
        1, frames, segment_frame, (matmul(first_update, columns), first_offset, noise_cov)
    )

    offset_rows = offset.shape[0] // panel_width
    distances = [1 << level for level in range(tm_devices.bit_length()) if 1 << level < tm_devices]
    chain_full = full_columns(chain_cols)
    cov_sent = []
    for position, stride in enumerate(distances):
        last = position == len(distances) - 1
        if last:
            sent = offset.reshape(offset_rows, panel_width)
        else:
            sent = jnp.concatenate([chain_cols, offset.reshape(offset_rows, panel_width)], axis=0)
        got = shifted(sent, "tm", stride)
        cov_sent.append(cov_cols)
        got_cov = shifted(cov_cols, "tm", stride)
        cov_got = got_cov
        got_offset = got[got.shape[0] - offset_rows:].reshape(node_count)
        active = segment >= stride
        chain_rows = lax.dynamic_slice_in_dim(chain_full, panel_start, panel_width, 0)
        earlier_cov = full_columns(got_cov)
        new_cov = matmul(chain_full, matmul(earlier_cov, chain_rows.T)) + cov_cols
        new_offset = matmul(chain_full, got_offset) + offset
        cov_cols = jnp.where(active, new_cov, cov_cols)
        offset = jnp.where(active, new_offset, offset)
        if not last:
            new_chain = matmul(chain_full, got[: node_count])
            chain_cols = jnp.where(active, new_chain, chain_cols)
            chain_full = full_columns(chain_cols)
    cov_out = cov_cols[None]
    mean_start = jnp.where(segment == 0, initial_mean, shifted(offset, "tm", 1))
    ties = cov_sent[-3:] + [cov_got]
    if ties:
        mean_start, _ = lax.optimization_barrier((mean_start, ties[0]))

    scale_rows = jnp.repeat(frame_scale, block_size, axis=1)
    mean_stack = []
    pred_stack = []
    mean_now = mean_start
    for frame in range(frames):
        predicted = scale_rows[frame] * matmul(coupling, mean_now)
        mean_now = damping * predicted + inject[frame]
        mean_stack.append(mean_now)
        pred_stack.append(predicted)

    def smooth_pass(bracket):
        smooth = [None] * frames
        for frame in reversed(range(frames)):
            smooth[frame] = mean_stack[frame] + matmul(smoother_gain, bracket)
            bracket = smooth[frame] - pred_stack[frame]
        return bracket, jnp.stack(smooth)

    own_bracket, _ = smooth_pass(jnp.zeros_like(initial_mean))
    squares = [matrix_power(smoother_gain, frames)]
    powers = {}

    def power(exponent):
        if exponent not in powers:
            result = None
            bit = 0
            while exponent >> bit:
                while len(squares) <= bit:
                    squares.append(matmul(squares[-1], squares[-1]))
                if (exponent >> bit) & 1:
                    result = squares[bit] if result is None else matmul(result, squares[bit])
                bit += 1
            powers[exponent] = result
        return powers[exponent]

    suffix = None
    for step in range(1, 5):
        if step < tm_devices:
            term = shifted(own_bracket, "tm", -step)
            if step > 1:
                term = matmul(power(step - 1), term)
            suffix = term if suffix is None else suffix + term
    width = 4
    tie = 1
    while width < tm_devices - 1:
        if tie < len(ties):
            suffix, _ = lax.optimization_barrier((suffix, ties[tie]))
        tie += 1
        terms = []
        for multiple in range(1, 4):
            if multiple * width < tm_devices:
                terms.append((multiple * width, shifted(suffix, "tm", -multiple * width)))
        for stride, received in terms:
            suffix = suffix + matmul(power(stride), received)
        width *= 4
    _, smoothed = smooth_pass(suffix)
    return (cov_out, lax.dynamic_slice_in_dim(smoothed, panel_start, panel_width, 1))


def solution(mesh):
    return jax.shard_map(
        local,
        mesh=mesh,
        in_specs=(P(), P(), P(), P("tm", None), P(), P(), P("tm", None), P(None, "rows"), P(), P()),
        out_specs=(P("tm", None, "rows"), P("tm", "rows")),
        check_vma=False,
    )
```

```python
import jax
import jax.numpy as jnp
from jax import lax
from jax.sharding import PartitionSpec as P

HIGHEST_PRECISION = lax.Precision.HIGHEST


def shifted(value, axis, steps):
    count = lax.axis_size(axis)
    leading, last = (max(0, -steps), min(count, count - steps))
    return lax.ppermute(value, axis, [(source, source + steps) for source in range(leading, last)])


def matmul(left, right):
    return jnp.dot(left, right, precision=HIGHEST_PRECISION, preferred_element_type=jnp.float32)


def full_columns(panel):
    count = lax.axis_size("rows")
    if count != 2:
        return lax.all_gather(panel, "rows", axis=1, tiled=True)
    other = lax.ppermute(panel, "rows", [(0, 1), (1, 0)])
    first = lax.axis_index("rows") == 0
    left = jnp.where(first, panel, other)
    right = jnp.where(first, other, panel)
    return jnp.concatenate([left, right], axis=1)


def build_coupling(band_blocks, band_offsets, retention):
    block_count = band_blocks.shape[0]
    block_size = band_blocks.shape[2]
    totals = jnp.sum(band_blocks, axis=(1, 3))
    normed = band_blocks / totals[:, None, :, None]
    placement = (
        band_offsets[:, :, None] == jnp.arange(block_count, dtype=jnp.int32)[None, None, :]
    ).astype(jnp.float32)
    spread_matrix = jnp.einsum("ibj,ibac->iajc", placement, normed, precision=HIGHEST_PRECISION)
    spread_matrix = spread_matrix.reshape(block_count * block_size, block_count * block_size)
    return (1.0 - retention)[:, None] * spread_matrix + jnp.diag(retention)


def matrix_power(square, exponent):
    result = None
    factor = square
    while exponent > 0:
        if exponent % 2 == 1:
            result = factor
        exponent = exponent // 2
        if exponent > 0:
            factor = matmul(factor, factor)
    return result


def local(
    band_blocks,
    band_offsets,
    retention,
    frame_scale,
    sensor_index,
    sensor_gain,
    readings,
    noise_cov,
    initial_mean,
    smoother_gain,
):
    node_count = retention.shape[0]
    block_size = band_blocks.shape[2]
    frames = readings.shape[0]
    panel_width = noise_cov.shape[1]
    tm_devices = lax.axis_size("tm")
    segment = lax.axis_index("tm")
    panel_start = lax.axis_index("rows") * panel_width
    coupling = build_coupling(band_blocks, band_offsets, retention)
    sensor_hit = (sensor_index[:, None] == jnp.arange(node_count, dtype=jnp.int32)[None, :]).astype(
        jnp.float32
    )
    damping = 1.0 - matmul(sensor_gain, sensor_hit)
    inject = matmul(readings * sensor_gain[None, :], sensor_hit)
    anchor = jnp.where(segment == 0, initial_mean, jnp.zeros_like(initial_mean))

    def transition(frame):
        scale_row = lax.dynamic_index_in_dim(frame_scale, frame, 0, keepdims=False)
        return jnp.repeat(scale_row, block_size)[:, None] * coupling

    def injected(frame):
        return lax.dynamic_index_in_dim(inject, frame, 0, keepdims=False)

    first_update = damping[:, None] * transition(0)
    first_offset = matmul(first_update, anchor) + inject[0]
    columns = (
        jnp.arange(node_count, dtype=jnp.int32)[:, None]
        == panel_start + jnp.arange(panel_width, dtype=jnp.int32)[None, :]
    ).astype(jnp.float32)

    def segment_frame(frame, carry):
        chain_cols, offset, cov_cols = carry
        update = damping[:, None] * transition(frame)
        gathered = full_columns(cov_cols)
        update_rows = lax.dynamic_slice_in_dim(update, panel_start, panel_width, 0)
        cov_cols = matmul(update, matmul(gathered, update_rows.T)) + noise_cov
        return (matmul(update, chain_cols), matmul(update, offset) + injected(frame), cov_cols)

    chain_cols, offset, cov_cols = lax.fori_loop(
        1, frames, segment_frame, (matmul(first_update, columns), first_offset, noise_cov)
    )

    offset_rows = offset.shape[0] // panel_width
    distances = [1 << level for level in range(tm_devices.bit_length()) if 1 << level < tm_devices]
    chain_full = full_columns(chain_cols)
    cov_sent = []
    for position, stride in enumerate(distances):
        last = position == len(distances) - 1
        if last:
            sent = offset.reshape(offset_rows, panel_width)
        else:
            sent = jnp.concatenate([chain_cols, offset.reshape(offset_rows, panel_width)], axis=0)
        got = shifted(sent, "tm", stride)
        cov_sent.append(cov_cols)
        got_cov = shifted(cov_cols, "tm", stride)
        cov_got = got_cov
        got_offset = got[got.shape[0] - offset_rows:].reshape(node_count)
        active = segment >= stride
        chain_rows = lax.dynamic_slice_in_dim(chain_full, panel_start, panel_width, 0)
        earlier_cov = full_columns(got_cov)
        new_cov = matmul(chain_full, matmul(earlier_cov, chain_rows.T)) + cov_cols
        new_offset = matmul(chain_full, got_offset) + offset
        cov_cols = jnp.where(active, new_cov, cov_cols)
        offset = jnp.where(active, new_offset, offset)
        if not last:
            new_chain = matmul(chain_full, got[: node_count])
            chain_cols = jnp.where(active, new_chain, chain_cols)
            chain_full = full_columns(chain_cols)
    cov_out = cov_cols[None]
    mean_start = jnp.where(segment == 0, initial_mean, shifted(offset, "tm", 1))
    ties = cov_sent[-3:] + [cov_got]
    if ties:
        mean_start, _ = lax.optimization_barrier((mean_start, ties[0]))

    scale_rows = jnp.repeat(frame_scale, block_size, axis=1)
    mean_stack = []
    pred_stack = []
    mean_now = mean_start
    for frame in range(frames):
        predicted = scale_rows[frame] * matmul(coupling, mean_now)
        mean_now = damping * predicted + inject[frame]
        mean_stack.append(mean_now)
        pred_stack.append(predicted)

    gain_powers = [smoother_gain]
    for _ in range(1, frames):
        gain_powers.append(matmul(gain_powers[-1], smoother_gain))
    stacked = jnp.concatenate(gain_powers, axis=0)
    gaps = jnp.stack([mean_stack[j] - pred_stack[j] for j in range(frames)], axis=1)
    moved = matmul(stacked, gaps).reshape(frames, node_count, frames)
    within = []
    for k in range(frames):
        term = mean_stack[k]
        for j in range(k + 1, frames):
            term = term + moved[j - k - 1, :, j]
        within.append(term)

    def smooth_pass(bracket):
        carried = matmul(stacked, bracket).reshape(frames, node_count)
        smooth = jnp.stack([within[k] + carried[frames - k - 1] for k in range(frames)])
        return smooth

    own_bracket = within[0] - pred_stack[0]
    squares = [gain_powers[frames - 1]]
    powers = {}

    def power(exponent):
        if exponent not in powers:
            result = None
            bit = 0
            while exponent >> bit:
                while len(squares) <= bit:
                    squares.append(matmul(squares[-1], squares[-1]))
                if (exponent >> bit) & 1:
                    result = squares[bit] if result is None else matmul(result, squares[bit])
                bit += 1
            powers[exponent] = result
        return powers[exponent]

    suffix = None
    for step in range(1, 5):
        if step < tm_devices:
            term = shifted(own_bracket, "tm", -step)
            if step > 1:
                term = matmul(power(step - 1), term)
            suffix = term if suffix is None else suffix + term
    width = 4
    tie = 1
    while width < tm_devices - 1:
        if tie < len(ties):
            suffix, _ = lax.optimization_barrier((suffix, ties[tie]))
        tie += 1
        terms = []
        for multiple in range(1, 4):
            if multiple * width < tm_devices:
                terms.append((multiple * width, shifted(suffix, "tm", -multiple * width)))
        for stride, received in terms:
            suffix = suffix + matmul(power(stride), received)
        width *= 4
    smoothed = smooth_pass(suffix)
    return (cov_out, lax.dynamic_slice_in_dim(smoothed, panel_start, panel_width, 1))


def solution(mesh):
    return jax.shard_map(
        local,
        mesh=mesh,
        in_specs=(P(), P(), P(), P("tm", None), P(), P(), P("tm", None), P(None, "rows"), P(), P()),
        out_specs=(P("tm", None, "rows"), P("tm", "rows")),
        check_vma=False,
    )
```

```python
import jax
import jax.numpy as jnp
from jax import lax
from jax.sharding import PartitionSpec as P

HIGHEST_PRECISION = lax.Precision.HIGHEST


def shifted(value, axis, steps):
    count = lax.axis_size(axis)
    leading, last = (max(0, -steps), min(count, count - steps))
    return lax.ppermute(value, axis, [(source, source + steps) for source in range(leading, last)])


def matmul(left, right):
    return jnp.dot(left, right, precision=HIGHEST_PRECISION, preferred_element_type=jnp.float32)


def full_columns(panel):
    count = lax.axis_size("rows")
    if count != 2:
        return lax.all_gather(panel, "rows", axis=1, tiled=True)
    other = lax.ppermute(panel, "rows", [(0, 1), (1, 0)])
    first = lax.axis_index("rows") == 0
    left = jnp.where(first, panel, other)
    right = jnp.where(first, other, panel)
    return jnp.concatenate([left, right], axis=1)


def build_coupling(band_blocks, band_offsets, retention):
    block_count = band_blocks.shape[0]
    block_size = band_blocks.shape[2]
    totals = jnp.sum(band_blocks, axis=(1, 3))
    normed = band_blocks / totals[:, None, :, None]
    placement = (
        band_offsets[:, :, None] == jnp.arange(block_count, dtype=jnp.int32)[None, None, :]
    ).astype(jnp.float32)
    spread_matrix = jnp.einsum("ibj,ibac->iajc", placement, normed, precision=HIGHEST_PRECISION)
    spread_matrix = spread_matrix.reshape(block_count * block_size, block_count * block_size)
    return (1.0 - retention)[:, None] * spread_matrix + jnp.diag(retention)


def matrix_power(square, exponent):
    result = None
    factor = square
    while exponent > 0:
        if exponent % 2 == 1:
            result = factor
        exponent = exponent // 2
        if exponent > 0:
            factor = matmul(factor, factor)
    return result


def local(
    band_blocks,
    band_offsets,
    retention,
    frame_scale,
    sensor_index,
    sensor_gain,
    readings,
    noise_cov,
    initial_mean,
    smoother_gain,
):
    node_count = retention.shape[0]
    block_size = band_blocks.shape[2]
    frames = readings.shape[0]
    panel_width = noise_cov.shape[1]
    tm_devices = lax.axis_size("tm")
    segment = lax.axis_index("tm")
    panel_start = lax.axis_index("rows") * panel_width
    coupling = build_coupling(band_blocks, band_offsets, retention)
    sensor_hit = (sensor_index[:, None] == jnp.arange(node_count, dtype=jnp.int32)[None, :]).astype(
        jnp.float32
    )
    damping = 1.0 - matmul(sensor_gain, sensor_hit)
    inject = matmul(readings * sensor_gain[None, :], sensor_hit)
    anchor = jnp.where(segment == 0, initial_mean, jnp.zeros_like(initial_mean))

    def transition(frame):
        scale_row = lax.dynamic_index_in_dim(frame_scale, frame, 0, keepdims=False)
        return jnp.repeat(scale_row, block_size)[:, None] * coupling

    def injected(frame):
        return lax.dynamic_index_in_dim(inject, frame, 0, keepdims=False)

    first_update = damping[:, None] * transition(0)
    first_offset = matmul(first_update, anchor) + inject[0]
    columns = (
        jnp.arange(node_count, dtype=jnp.int32)[:, None]
        == panel_start + jnp.arange(panel_width, dtype=jnp.int32)[None, :]
    ).astype(jnp.float32)

    def segment_frame(frame, carry):
        chain_cols, offset, cov_cols = carry
        update = damping[:, None] * transition(frame)
        gathered = full_columns(cov_cols)
        update_rows = lax.dynamic_slice_in_dim(update, panel_start, panel_width, 0)
        cov_cols = matmul(update, matmul(gathered, update_rows.T)) + noise_cov
        return (matmul(update, chain_cols), matmul(update, offset) + injected(frame), cov_cols)

    carry = (matmul(first_update, columns), first_offset, noise_cov)
    for frame in range(1, frames):
        carry = segment_frame(frame, carry)
    chain_cols, offset, cov_cols = carry

    offset_rows = offset.shape[0] // panel_width
    distances = [1 << level for level in range(tm_devices.bit_length()) if 1 << level < tm_devices]
    chain_full = full_columns(chain_cols)
    cov_sent = []
    for position, stride in enumerate(distances):
        last = position == len(distances) - 1
        if last:
            sent = offset.reshape(offset_rows, panel_width)
        else:
            sent = jnp.concatenate([chain_cols, offset.reshape(offset_rows, panel_width)], axis=0)
        got = shifted(sent, "tm", stride)
        cov_sent.append(cov_cols)
        got_cov = shifted(cov_cols, "tm", stride)
        cov_got = got_cov
        got_offset = got[got.shape[0] - offset_rows:].reshape(node_count)
        active = segment >= stride
        chain_rows = lax.dynamic_slice_in_dim(chain_full, panel_start, panel_width, 0)
        earlier_cov = full_columns(got_cov)
        new_cov = matmul(chain_full, matmul(earlier_cov, chain_rows.T)) + cov_cols
        new_offset = matmul(chain_full, got_offset) + offset
        cov_cols = jnp.where(active, new_cov, cov_cols)
        offset = jnp.where(active, new_offset, offset)
        if not last:
            new_chain = matmul(chain_full, got[: node_count])
            chain_cols = jnp.where(active, new_chain, chain_cols)
            chain_full = full_columns(chain_cols)
    cov_out = cov_cols[None]
    mean_start = jnp.where(segment == 0, initial_mean, shifted(offset, "tm", 1))
    ties = cov_sent[-3:] + [cov_got]
    if ties:
        mean_start, _ = lax.optimization_barrier((mean_start, ties[0]))

    scale_rows = jnp.repeat(frame_scale, block_size, axis=1)
    mean_stack = []
    pred_stack = []
    mean_now = mean_start
    for frame in range(frames):
        predicted = scale_rows[frame] * matmul(coupling, mean_now)
        mean_now = damping * predicted + inject[frame]
        mean_stack.append(mean_now)
        pred_stack.append(predicted)

    def smooth_pass(bracket):
        smooth = [None] * frames
        for frame in reversed(range(frames)):
            smooth[frame] = mean_stack[frame] + matmul(smoother_gain, bracket)
            bracket = smooth[frame] - pred_stack[frame]
        return bracket, jnp.stack(smooth)

    own_bracket, _ = smooth_pass(jnp.zeros_like(initial_mean))
    squares = [matrix_power(smoother_gain, frames)]
    powers = {}

    def power(exponent):
        if exponent not in powers:
            result = None
            bit = 0
            while exponent >> bit:
                while len(squares) <= bit:
                    squares.append(matmul(squares[-1], squares[-1]))
                if (exponent >> bit) & 1:
                    result = squares[bit] if result is None else matmul(result, squares[bit])
                bit += 1
            powers[exponent] = result
        return powers[exponent]

    suffix = None
    for step in range(1, 5):
        if step < tm_devices:
            term = shifted(own_bracket, "tm", -step)
            if step > 1:
                term = matmul(power(step - 1), term)
            suffix = term if suffix is None else suffix + term
    width = 4
    tie = 1
    while width < tm_devices - 1:
        if tie < len(ties):
            suffix, _ = lax.optimization_barrier((suffix, ties[tie]))
        tie += 1
        terms = []
        for multiple in range(1, 4):
            if multiple * width < tm_devices:
                terms.append((multiple * width, shifted(suffix, "tm", -multiple * width)))
        for stride, received in terms:
            suffix = suffix + matmul(power(stride), received)
        width *= 4
    _, smoothed = smooth_pass(suffix)
    return (cov_out, lax.dynamic_slice_in_dim(smoothed, panel_start, panel_width, 1))


def solution(mesh):
    return jax.shard_map(
        local,
        mesh=mesh,
        in_specs=(P(), P(), P(), P("tm", None), P(), P(), P("tm", None), P(None, "rows"), P(), P()),
        out_specs=(P("tm", None, "rows"), P("tm", "rows")),
        check_vma=False,
    )
```
